512 devices in a mesh: grp: 64 (over x, y, z_lo), mem: 8 (over z_hi, core).
Axes of the slice: x: 4, y: 8, z: 8 (z_hi: 4, z_lo: 2; z = z_hi * 2 + z_lo), core: 2. Of those that a mesh axis runs over, the one named last changes fastest.
Arguments:
- raw_traces: float32 [4096, 6030], P(('grp', 'mem')), may hold values from -6 to 6
Outputs:
- correlations: bfloat16 [4096, 512, 401], P(('grp', 'mem'))
The draws below stay inside these ranges and needn't reach their ends.
All inputs are finite; a program needn't handle non-finite values.
Results may differ from the reference program's by a relative error of at most 0.0063.
Values may be sent and summed in bfloat16 or wider, within the bound.
No kernel may reach another device: no remote copies, remote signals or barrier semaphores. Data moves between devices by JAX's collectives and lax.ppermute only.
A program may use at most 64 MiB of HBM per device.

```python
import math
import jax
import jax.numpy as jnp
from jax import lax

CH_DEV = 8
WINDOWS = 2
WLEN = 1500
NFREQ = 384
TAPS = 32
MAXLAG = 200
LAGS = 401
RAWLEN = 6030
CHANNELS = 4096


def steps_of(key, shape, cuts, least, largest):
    loudness, own = 1.0, jax.random.fold_in(key, 6)
    for dim, parts in cuts:
        steps = jnp.exp(jax.random.uniform(jax.random.fold_in(own, dim), (parts,), jnp.float32, least / len(cuts), largest / len(cuts)))
        loudness = loudness * jnp.repeat(steps, shape[dim] // parts).reshape([-1 if axis == dim else 1 for axis in range(len(shape))])
    return loudness


def normal_values(key, shape, spread, reach, pieces=(), held_as=jnp.bfloat16):
    entries = jax.random.normal(key, shape, jnp.float32) * spread
    if len(pieces) > 0:
        entries = steps_of(key, shape, pieces, -0.22, 0.18) * entries
    return jnp.clip(entries, min=-reach, max=reach).astype(held_as)


def setup_inputs(seed: int = 0) -> dict:
    seeds = jax.random.split(jax.random.key(seed), 2)
    return {
        "raw_traces": normal_values(seeds[0], (CHANNELS, RAWLEN), 1.0, 6.0, ((0, 512),), jnp.float32),
    }


def lowpass(taps):
    k = jnp.arange(taps).astype(jnp.float32)
    centre = (taps - 1) / 2.0
    window = 0.5 - 0.5 * jnp.cos(2.0 * math.pi * (k + 0.5) / taps)
    return 0.5 * jnp.sinc((k - centre) * 0.5) * window

def forward_table():
    times = jnp.arange(WLEN).astype(jnp.int32)
    bins = jnp.arange(1, NFREQ + 1).astype(jnp.int32)
    phase = times[:, None] * bins[None, :] % WLEN
    angle = 2.0 * math.pi * phase.astype(jnp.float32) / WLEN
    return jnp.concatenate([jnp.cos(angle), -jnp.sin(angle)], axis=1)

def inverse_table():
    bins = jnp.arange(1, NFREQ + 1).astype(jnp.int32)
    shifts = jnp.arange(LAGS).astype(jnp.int32) - MAXLAG
    phase = jnp.mod(bins[:, None] * shifts[None, :], WLEN)
    angle = 2.0 * math.pi * phase.astype(jnp.float32) / WLEN
    return jnp.concatenate([jnp.cos(angle), -jnp.sin(angle)], axis=0).astype(jnp.bfloat16)

def whiten(raw_traces):
    count = raw_traces.shape[0]
    total = WINDOWS * WLEN
    filt = lowpass(TAPS)
    decimated = jnp.zeros((count, total), jnp.float32)
    for k in range(TAPS):
        piece = lax.slice(raw_traces, (0, k), (count, k + 2 * total - 1), (1, 2))
        decimated = decimated + filt[k] * piece
    frames = decimated.reshape(count * WINDOWS, WLEN)
    spec = jnp.dot(frames, forward_table(), precision=lax.Precision.HIGHEST, preferred_element_type=jnp.float32)
    spec_re = spec[:, :NFREQ]
    spec_im = spec[:, NFREQ:]
    power = spec_re * spec_re + spec_im * spec_im
    level = 0.01 * lax.optimization_barrier(jnp.mean(power, axis=1, keepdims=True))
    factor = 1.0 / jnp.sqrt(power + level + 1e-06)
    white = jnp.concatenate([spec_re * factor, spec_im * factor], axis=1)
    return white.astype(jnp.bfloat16).reshape(count, WINDOWS, 2 * NFREQ)

def reference(raw_traces):
    white = whiten(raw_traces)
    sources = white[::CH_DEV]
    recv = white.astype(jnp.float32)
    recv_re = recv[:, :, :NFREQ]
    recv_im = recv[:, :, NFREQ:]
    table = inverse_table().astype(jnp.float32)
    scale = 1.0 / math.sqrt(WINDOWS * NFREQ)

    def one_source(source):
        src = source.astype(jnp.float32)
        src_re = src[None, :, :NFREQ]
        src_im = src[None, :, NFREQ:]
        cross_re = lax.optimization_barrier(jnp.sum(recv_re * src_re + recv_im * src_im, axis=1))
        cross_im = lax.optimization_barrier(jnp.sum(recv_im * src_re - recv_re * src_im, axis=1))
        cross = jnp.concatenate([cross_re, cross_im], axis=1).astype(jnp.bfloat16).astype(jnp.float32)
        corr = jnp.dot(cross, table, preferred_element_type=jnp.float32) * scale
        return corr.astype(jnp.bfloat16)
    stacked = lax.map(one_source, sources)
    return jnp.transpose(stacked, (1, 0, 2))
```

```python
import functools
import math

import numpy as np
import jax
import jax.numpy as jnp
from jax import lax
from jax.experimental import pallas as pl
from jax.sharding import PartitionSpec as P

CH_DEV = 8
WINDOWS = 2
WLEN = 1500
NFREQ = 384
TAPS = 32
MAXLAG = 200


def lowpass(taps):
    k = np.arange(taps, dtype=np.float64)
    centre = (taps - 1) / 2.0
    window = 0.5 - 0.5 * np.cos(2.0 * math.pi * (k + 0.5) / taps)
    return 0.5 * np.sinc((k - centre) * 0.5) * window


def forward_table(wlen, nfreq):
    times = np.arange(wlen, dtype=np.int64)
    bins = np.arange(1, nfreq + 1, dtype=np.int64)
    angle = 2.0 * math.pi * ((times[:, None] * bins[None, :]) % wlen) / wlen
    return np.concatenate([np.cos(angle), -np.sin(angle)], axis=1)


def filtered_table(wlen, nfreq, taps):
    filt = lowpass(taps)
    dft = forward_table(wlen, nfreq)
    table = np.zeros((2 * wlen + taps - 2, 2 * nfreq), np.float64)
    for k in range(taps):
        table[k : k + 2 * wlen : 2] += filt[k] * dft
    return table.astype(np.float32)


def inverse_table(wlen, nfreq, maxlag):
    bins = np.arange(1, nfreq + 1, dtype=np.int64)
    shifts = np.arange(2 * maxlag + 1, dtype=np.int64) - maxlag
    phase = np.mod(bins[:, None] * shifts[None, :], wlen).astype(np.float32)
    angle = np.float32(2.0 * math.pi) * phase / np.float32(wlen)
    table = np.concatenate([np.cos(angle), -np.sin(angle)], axis=0).astype(np.float32)
    padded = np.zeros((table.shape[0], -(-table.shape[1] // 128) * 128), np.float32)
    padded[:, : table.shape[1]] = table
    return jnp.asarray(padded).astype(jnp.bfloat16)


def whiten(raw_traces):
    count = raw_traces.shape[0]
    span = 2 * WLEN + TAPS - 2
    windows = jnp.stack(
        [raw_traces[:, w * 2 * WLEN : w * 2 * WLEN + span] for w in range(WINDOWS)], axis=1
    ).reshape(count * WINDOWS, span)
    spec = jnp.dot(
        windows,
        jnp.asarray(filtered_table(WLEN, NFREQ, TAPS)),
        precision=lax.Precision.HIGHEST,
        preferred_element_type=jnp.float32,
    )
    spec_re = spec[:, :NFREQ]
    spec_im = spec[:, NFREQ:]
    power = spec_re * spec_re + spec_im * spec_im
    level = 0.01 * jnp.mean(power, axis=1, keepdims=True)
    factor = 1.0 / jnp.sqrt(power + level + 1e-06)
    white = jnp.concatenate([spec_re * factor, spec_im * factor], axis=1)
    return white.astype(jnp.bfloat16).reshape(count, WINDOWS, 2 * NFREQ)


SRC_BLOCK = 128


def correlate_kernel(scale, recv_ref, src_ref, table_ref, out_ref):
    nf = NFREQ
    src = src_ref[...].astype(jnp.float32)
    s_re0, s_im0 = src[:, 0:nf], src[:, nf : 2 * nf]
    s_re1, s_im1 = src[:, 2 * nf : 3 * nf], src[:, 3 * nf : 4 * nf]
    t_re = table_ref[0:nf, :]
    t_im = table_ref[nf : 2 * nf, :]
    lags = out_ref.shape[2]
    for c in range(out_ref.shape[0]):
        a = recv_ref[c : c + 1, :].astype(jnp.float32)
        a_re0, a_im0 = a[:, 0:nf], a[:, nf : 2 * nf]
        a_re1, a_im1 = a[:, 2 * nf : 3 * nf], a[:, 3 * nf : 4 * nf]
        c_re = (a_re0 * s_re0 + a_im0 * s_im0) + (a_re1 * s_re1 + a_im1 * s_im1)
        c_im = (a_im0 * s_re0 - a_re0 * s_im0) + (a_im1 * s_re1 - a_re1 * s_im1)
        acc = jnp.dot(c_re.astype(jnp.bfloat16), t_re, preferred_element_type=jnp.float32)
        acc = acc + jnp.dot(c_im.astype(jnp.bfloat16), t_im, preferred_element_type=jnp.float32)
        out_ref[c] = (acc[:, :lags] * scale).astype(out_ref.dtype)


def correlate(recv, src, table, lags):
    count, width = recv.shape[0], src.shape[0]
    block = min(SRC_BLOCK, width)
    scale = 1.0 / math.sqrt(WINDOWS * NFREQ)
    flops = 2 * count * width * table.shape[0] * table.shape[1] + 16 * count * width * NFREQ
    bytes_accessed = 2 * (recv.size + src.size + table.size + count * width * lags)
    return pl.pallas_call(
        functools.partial(correlate_kernel, scale),
        grid=(width // block,),
        in_specs=[
            pl.BlockSpec((count, recv.shape[1]), lambda j: (0, 0)),
            pl.BlockSpec((block, src.shape[1]), lambda j: (j, 0)),
            pl.BlockSpec(table.shape, lambda j: (0, 0)),
        ],
        out_specs=pl.BlockSpec((count, block, lags), lambda j: (0, j, 0)),
        out_shape=jax.ShapeDtypeStruct((count, width, lags), jnp.bfloat16),
        cost_estimate=pl.CostEstimate(flops=flops, transcendentals=0, bytes_accessed=bytes_accessed),
    )(recv, src, table)


def gather_sources(own_source):
    axes = ("grp", "mem")
    total = 1
    for name in axes:
        total *= lax.axis_size(name)
    copies = jnp.broadcast_to(own_source, (total,) + own_source.shape[1:])
    return lax.all_to_all(copies, axes, 0, 0, tiled=True)


def on_device(raw_traces):
    white = whiten(raw_traces)
    count = white.shape[0]
    sources = gather_sources(white[:1])
    recv = white.reshape(count, WINDOWS * 2 * NFREQ)
    src = sources.reshape(sources.shape[0], WINDOWS * 2 * NFREQ)
    return correlate(recv, src, inverse_table(WLEN, NFREQ, MAXLAG), 2 * MAXLAG + 1)


def solution(mesh):
    return jax.shard_map(
        on_device,
        mesh=mesh,
        in_specs=(P(("grp", "mem"), None),),
        out_specs=P(("grp", "mem"), None, None),
        check_vma=False,
    )
```

```python
import functools
import math

import numpy as np
import jax
import jax.numpy as jnp
from jax import lax
from jax.experimental import pallas as pl
from jax.sharding import PartitionSpec as P

CH_DEV = 8
WINDOWS = 2
WLEN = 1500
NFREQ = 384
TAPS = 32
MAXLAG = 200


def lowpass(taps):
    k = np.arange(taps, dtype=np.float64)
    centre = (taps - 1) / 2.0
    window = 0.5 - 0.5 * np.cos(2.0 * math.pi * (k + 0.5) / taps)
    return 0.5 * np.sinc((k - centre) * 0.5) * window


def forward_table(wlen, nfreq):
    times = np.arange(wlen, dtype=np.int64)
    bins = np.arange(1, nfreq + 1, dtype=np.int64)
    angle = 2.0 * math.pi * ((times[:, None] * bins[None, :]) % wlen) / wlen
    return np.concatenate([np.cos(angle), -np.sin(angle)], axis=1)


def filtered_table(wlen, nfreq, taps):
    filt = lowpass(taps)
    dft = forward_table(wlen, nfreq)
    table = np.zeros((2 * wlen + taps - 2, 2 * nfreq), np.float64)
    for k in range(taps):
        table[k : k + 2 * wlen : 2] += filt[k] * dft
    return table.astype(np.float32)


def inverse_table(wlen, nfreq, maxlag):
    bins = np.arange(1, nfreq + 1, dtype=np.int64)
    shifts = np.arange(2 * maxlag + 1, dtype=np.int64) - maxlag
    phase = np.mod(bins[:, None] * shifts[None, :], wlen).astype(np.float32)
    angle = np.float32(2.0 * math.pi) * phase / np.float32(wlen)
    table = np.concatenate([np.cos(angle), -np.sin(angle)], axis=0).astype(np.float32)
    padded = np.zeros((-(-table.shape[1] // 16) * 16, table.shape[0]), np.float32)
    padded[: table.shape[1]] = table.T
    return jnp.asarray(padded).astype(jnp.bfloat16)


def whiten(raw_traces):
    count = raw_traces.shape[0]
    span = 2 * WLEN + TAPS - 2
    windows = jnp.stack(
        [raw_traces[:, w * 2 * WLEN : w * 2 * WLEN + span] for w in range(WINDOWS)], axis=1
    ).reshape(count * WINDOWS, span)
    spec = jnp.dot(
        windows,
        jnp.asarray(filtered_table(WLEN, NFREQ, TAPS)),
        precision=lax.Precision.HIGH,
        preferred_element_type=jnp.float32,
    )
    spec_re = spec[:, :NFREQ]
    spec_im = spec[:, NFREQ:]
    power = spec_re * spec_re + spec_im * spec_im
    level = 0.01 * jnp.mean(power, axis=1, keepdims=True)
    factor = 1.0 / jnp.sqrt(power + level + 1e-06)
    white = jnp.concatenate([spec_re * factor, spec_im * factor], axis=1)
    return white.astype(jnp.bfloat16).reshape(count, WINDOWS, 2 * NFREQ)


SRC_BLOCK = 128


def correlate_kernel(scale, recv_ref, src_ref, table_ref, out_ref):
    nf = NFREQ
    src = src_ref[...].astype(jnp.float32)
    s_re0, s_im0 = src[0:nf], src[nf : 2 * nf]
    s_re1, s_im1 = src[2 * nf : 3 * nf], src[3 * nf : 4 * nf]
    t_re = table_ref[:, 0:nf]
    t_im = table_ref[:, nf : 2 * nf]
    lags = out_ref.shape[0]
    for c in range(out_ref.shape[1]):
        a = recv_ref[:, c : c + 1].astype(jnp.float32)
        a_re0, a_im0 = a[0:nf], a[nf : 2 * nf]
        a_re1, a_im1 = a[2 * nf : 3 * nf], a[3 * nf : 4 * nf]
        c_re = (a_re0 * s_re0 + a_im0 * s_im0) + (a_re1 * s_re1 + a_im1 * s_im1)
        c_im = (a_im0 * s_re0 - a_re0 * s_im0) + (a_im1 * s_re1 - a_re1 * s_im1)
        acc = jnp.dot(t_re, c_re.astype(jnp.bfloat16), preferred_element_type=jnp.float32)
        acc = acc + jnp.dot(t_im, c_im.astype(jnp.bfloat16), preferred_element_type=jnp.float32)
        out_ref[:, c, :] = (acc[:lags] * scale).astype(out_ref.dtype)


def correlate(recv_t, src_t, table_t, lags):
    count, width = recv_t.shape[1], src_t.shape[1]
    block = min(SRC_BLOCK, width)
    scale = 1.0 / math.sqrt(WINDOWS * NFREQ)
    flops = 2 * count * width * table_t.shape[0] * table_t.shape[1] + 16 * count * width * NFREQ
    bytes_accessed = 2 * (recv_t.size + src_t.size + table_t.size + count * width * lags)
    return pl.pallas_call(
        functools.partial(correlate_kernel, scale),
        grid=(width // block,),
        in_specs=[
            pl.BlockSpec(recv_t.shape, lambda j: (0, 0)),
            pl.BlockSpec((src_t.shape[0], block), lambda j: (0, j)),
            pl.BlockSpec(table_t.shape, lambda j: (0, 0)),
        ],
        out_specs=pl.BlockSpec((lags, count, block), lambda j: (0, 0, j)),
        out_shape=jax.ShapeDtypeStruct((lags, count, width), jnp.bfloat16),
        cost_estimate=pl.CostEstimate(flops=flops, transcendentals=0, bytes_accessed=bytes_accessed),
    )(recv_t, src_t, table_t)


def gather_sources(own_source):
    axes = ("grp", "mem")
    total = 1
    for name in axes:
        total *= lax.axis_size(name)
    copies = jnp.broadcast_to(own_source, (total,) + own_source.shape[1:])
    return lax.all_to_all(copies, axes, 0, 0, tiled=True)


def on_device(raw_traces):
    white = whiten(raw_traces)
    count = white.shape[0]
    sources = gather_sources(white[:1])
    recv_t = white.reshape(count, WINDOWS * 2 * NFREQ).T
    src_t = sources.reshape(sources.shape[0], WINDOWS * 2 * NFREQ).T
    lags_first = correlate(recv_t, src_t, inverse_table(WLEN, NFREQ, MAXLAG), 2 * MAXLAG + 1)
    return jnp.transpose(lags_first, (1, 2, 0))


def solution(mesh):
    return jax.shard_map(
        on_device,
        mesh=mesh,
        in_specs=(P(("grp", "mem"), None),),
        out_specs=P(("grp", "mem"), None, None),
        check_vma=False,
    )
```

```python
import functools
import math

import numpy as np
import jax
import jax.numpy as jnp
from jax import lax
from jax.experimental import pallas as pl
from jax.sharding import PartitionSpec as P

CH_DEV = 8
WINDOWS = 2
WLEN = 1500
NFREQ = 384
TAPS = 32
MAXLAG = 200


def lowpass(taps):
    k = np.arange(taps, dtype=np.float64)
    centre = (taps - 1) / 2.0
    window = 0.5 - 0.5 * np.cos(2.0 * math.pi * (k + 0.5) / taps)
    return 0.5 * np.sinc((k - centre) * 0.5) * window


def forward_table(wlen, nfreq):
    times = np.arange(wlen, dtype=np.int64)
    bins = np.arange(1, nfreq + 1, dtype=np.int64)
    angle = 2.0 * math.pi * ((times[:, None] * bins[None, :]) % wlen) / wlen
    return np.concatenate([np.cos(angle), -np.sin(angle)], axis=1)


def filtered_table(wlen, nfreq, taps):
    filt = lowpass(taps)
    dft = forward_table(wlen, nfreq)
    table = np.zeros((2 * wlen + taps - 2, 2 * nfreq), np.float64)
    for k in range(taps):
        table[k : k + 2 * wlen : 2] += filt[k] * dft
    return table.astype(np.float32)


def inverse_table(wlen, nfreq, maxlag):
    bins = np.arange(1, nfreq + 1, dtype=np.int64)
    shifts = np.arange(2 * maxlag + 1, dtype=np.int64) - maxlag
    phase = np.mod(bins[:, None] * shifts[None, :], wlen).astype(np.float32)
    angle = np.float32(2.0 * math.pi) * phase / np.float32(wlen)
    table = np.concatenate([np.cos(angle), -np.sin(angle)], axis=0).astype(np.float32)
    padded = np.zeros((table.shape[0], -(-table.shape[1] // 128) * 128), np.float32)
    padded[:, : table.shape[1]] = table
    return jnp.asarray(padded).astype(jnp.bfloat16)


def whiten(raw_traces):
    count = raw_traces.shape[0]
    span = 2 * WLEN + TAPS - 2
    windows = jnp.stack(
        [raw_traces[:, w * 2 * WLEN : w * 2 * WLEN + span] for w in range(WINDOWS)], axis=1
    ).reshape(count * WINDOWS, span)
    spec = jnp.dot(
        windows,
        jnp.asarray(filtered_table(WLEN, NFREQ, TAPS)),
        precision=lax.Precision.HIGHEST,
        preferred_element_type=jnp.float32,
    )
    spec_re = spec[:, :NFREQ]
    spec_im = spec[:, NFREQ:]
    power = spec_re * spec_re + spec_im * spec_im
    level = 0.01 * jnp.mean(power, axis=1, keepdims=True)
    factor = 1.0 / jnp.sqrt(power + level + 1e-06)
    white = jnp.concatenate([spec_re * factor, spec_im * factor], axis=1)
    return white.astype(jnp.bfloat16).reshape(count, WINDOWS, 2 * NFREQ)


SRC_BLOCK = 128


def correlate_kernel(scale, recv_ref, src_ref, table_ref, out_ref):
    nf = NFREQ
    src = src_ref[...].astype(jnp.float32)
    s_re0, s_im0 = src[:, 0:nf], src[:, nf : 2 * nf]
    s_re1, s_im1 = src[:, 2 * nf : 3 * nf], src[:, 3 * nf : 4 * nf]
    t_re = table_ref[0:nf, :]
    t_im = table_ref[nf : 2 * nf, :]
    lags = out_ref.shape[1]
    for c in range(out_ref.shape[0]):
        a = recv_ref[c : c + 1, :].astype(jnp.float32)
        a_re0, a_im0 = a[:, 0:nf], a[:, nf : 2 * nf]
        a_re1, a_im1 = a[:, 2 * nf : 3 * nf], a[:, 3 * nf : 4 * nf]
        c_re = (a_re0 * s_re0 + a_im0 * s_im0) + (a_re1 * s_re1 + a_im1 * s_im1)
        c_im = (a_im0 * s_re0 - a_re0 * s_im0) + (a_im1 * s_re1 - a_re1 * s_im1)
        acc = jnp.dot(c_re.astype(jnp.bfloat16), t_re, preferred_element_type=jnp.float32)
        acc = acc + jnp.dot(c_im.astype(jnp.bfloat16), t_im, preferred_element_type=jnp.float32)
        out_ref[c] = (acc.T[:lags] * scale).astype(out_ref.dtype)


def correlate(recv, src, table, lags):
    count, width = recv.shape[0], src.shape[0]
    block = min(SRC_BLOCK, width)
    scale = 1.0 / math.sqrt(WINDOWS * NFREQ)
    flops = 2 * count * width * table.shape[0] * table.shape[1] + 16 * count * width * NFREQ
    bytes_accessed = 2 * (recv.size + src.size + table.size + count * width * lags)
    return pl.pallas_call(
        functools.partial(correlate_kernel, scale),
        grid=(width // block,),
        in_specs=[
            pl.BlockSpec((count, recv.shape[1]), lambda j: (0, 0)),
            pl.BlockSpec((block, src.shape[1]), lambda j: (j, 0)),
            pl.BlockSpec(table.shape, lambda j: (0, 0)),
        ],
        out_specs=pl.BlockSpec((count, lags, block), lambda j: (0, 0, j)),
        out_shape=jax.ShapeDtypeStruct((count, lags, width), jnp.bfloat16),
        cost_estimate=pl.CostEstimate(flops=flops, transcendentals=0, bytes_accessed=bytes_accessed),
    )(recv, src, table)


def gather_sources(own_source):
    axes = ("grp", "mem")
    total = 1
    for name in axes:
        total *= lax.axis_size(name)
    copies = jnp.broadcast_to(own_source, (total,) + own_source.shape[1:])
    return lax.all_to_all(copies, axes, 0, 0, tiled=True)


def on_device(raw_traces):
    white = whiten(raw_traces)
    count = white.shape[0]
    sources = gather_sources(white[:1])
    recv = white.reshape(count, WINDOWS * 2 * NFREQ)
    src = sources.reshape(sources.shape[0], WINDOWS * 2 * NFREQ)
    lags_mid = correlate(recv, src, inverse_table(WLEN, NFREQ, MAXLAG), 2 * MAXLAG + 1)
    return jnp.transpose(lags_mid, (0, 2, 1))


def solution(mesh):
    return jax.shard_map(
        on_device,
        mesh=mesh,
        in_specs=(P(("grp", "mem"), None),),
        out_specs=P(("grp", "mem"), None, None),
        check_vma=False,
    )
```

```python
import functools
import math

import numpy as np
import jax
import jax.numpy as jnp
from jax import lax
from jax.experimental import pallas as pl
from jax.sharding import PartitionSpec as P

CH_DEV = 8
WINDOWS = 2
WLEN = 1500
NFREQ = 384
TAPS = 32
MAXLAG = 200


def lowpass(taps):
    k = np.arange(taps, dtype=np.float64)
    centre = (taps - 1) / 2.0
    window = 0.5 - 0.5 * np.cos(2.0 * math.pi * (k + 0.5) / taps)
    return 0.5 * np.sinc((k - centre) * 0.5) * window


def forward_table(wlen, nfreq):
    times = np.arange(wlen, dtype=np.int64)
    bins = np.arange(1, nfreq + 1, dtype=np.int64)
    angle = 2.0 * math.pi * ((times[:, None] * bins[None, :]) % wlen) / wlen
    return np.concatenate([np.cos(angle), -np.sin(angle)], axis=1)


def filtered_table(wlen, nfreq, taps):
    filt = lowpass(taps)
    dft = forward_table(wlen, nfreq)
    table = np.zeros((2 * wlen + taps - 2, 2 * nfreq), np.float64)
    for k in range(taps):
        table[k : k + 2 * wlen : 2] += filt[k] * dft
    return table.astype(np.float32)


def inverse_table(wlen, nfreq, maxlag):
    bins = np.arange(1, nfreq + 1, dtype=np.int64)
    shifts = np.arange(2 * maxlag + 1, dtype=np.int64) - maxlag
    phase = np.mod(bins[:, None] * shifts[None, :], wlen).astype(np.float32)
    angle = np.float32(2.0 * math.pi) * phase / np.float32(wlen)
    table = np.concatenate([np.cos(angle), -np.sin(angle)], axis=0).astype(np.float32)
    padded = np.zeros((table.shape[0], -(-table.shape[1] // 128) * 128), np.float32)
    padded[:, : table.shape[1]] = table
    return jnp.asarray(padded).astype(jnp.bfloat16)


def whiten(raw_traces):
    count = raw_traces.shape[0]
    span = 2 * WLEN + TAPS - 2
    windows = jnp.stack(
        [raw_traces[:, w * 2 * WLEN : w * 2 * WLEN + span] for w in range(WINDOWS)], axis=1
    ).reshape(count * WINDOWS, span)
    spec = jnp.dot(
        windows,
        jnp.asarray(filtered_table(WLEN, NFREQ, TAPS)),
        precision=lax.Precision.HIGHEST,
        preferred_element_type=jnp.float32,
    )
    spec_re = spec[:, :NFREQ]
    spec_im = spec[:, NFREQ:]
    power = spec_re * spec_re + spec_im * spec_im
    level = 0.01 * jnp.mean(power, axis=1, keepdims=True)
    factor = 1.0 / jnp.sqrt(power + level + 1e-06)
    white = jnp.concatenate([spec_re * factor, spec_im * factor], axis=1)
    return white.astype(jnp.bfloat16).reshape(count, WINDOWS, 2 * NFREQ)


SRC_BLOCK = 128


def correlate_kernel(scale, recv_ref, src_ref, table_ref, out_ref):
    nf = NFREQ
    src = src_ref[...].astype(jnp.float32)
    s_re0, s_im0 = src[:, 0:nf], src[:, nf : 2 * nf]
    s_re1, s_im1 = src[:, 2 * nf : 3 * nf], src[:, 3 * nf : 4 * nf]
    count, lags, block = out_ref.shape
    parts_re, parts_im = [], []
    for c in range(count):
        a = recv_ref[c : c + 1, :].astype(jnp.float32)
        a_re0, a_im0 = a[:, 0:nf], a[:, nf : 2 * nf]
        a_re1, a_im1 = a[:, 2 * nf : 3 * nf], a[:, 3 * nf : 4 * nf]
        c_re = (a_re0 * s_re0 + a_im0 * s_im0) + (a_re1 * s_re1 + a_im1 * s_im1)
        c_im = (a_im0 * s_re0 - a_re0 * s_im0) + (a_im1 * s_re1 - a_re1 * s_im1)
        parts_re.append(c_re.astype(jnp.bfloat16))
        parts_im.append(c_im.astype(jnp.bfloat16))
    cross_re = jnp.concatenate(parts_re, axis=0)
    cross_im = jnp.concatenate(parts_im, axis=0)
    acc = jnp.dot(cross_re, table_ref[0:nf, :], preferred_element_type=jnp.float32)
    acc = acc + jnp.dot(cross_im, table_ref[nf : 2 * nf, :], preferred_element_type=jnp.float32)
    for c in range(count):
        rows = acc[c * block : (c + 1) * block]
        out_ref[c] = (rows.T[:lags] * scale).astype(out_ref.dtype)


def correlate(recv, src, table, lags):
    count, width = recv.shape[0], src.shape[0]
    block = min(SRC_BLOCK, width)
    scale = 1.0 / math.sqrt(WINDOWS * NFREQ)
    flops = 2 * count * width * table.shape[0] * table.shape[1] + 16 * count * width * NFREQ
    bytes_accessed = 2 * (recv.size + src.size + table.size + count * width * lags)
    return pl.pallas_call(
        functools.partial(correlate_kernel, scale),
        grid=(width // block,),
        in_specs=[
            pl.BlockSpec((count, recv.shape[1]), lambda j: (0, 0)),
            pl.BlockSpec((block, src.shape[1]), lambda j: (j, 0)),
            pl.BlockSpec(table.shape, lambda j: (0, 0)),
        ],
        out_specs=pl.BlockSpec((count, lags, block), lambda j: (0, 0, j)),
        out_shape=jax.ShapeDtypeStruct((count, lags, width), jnp.bfloat16),
        cost_estimate=pl.CostEstimate(flops=flops, transcendentals=0, bytes_accessed=bytes_accessed),
    )(recv, src, table)


def gather_sources(own_source):
    axes = ("grp", "mem")
    total = 1
    for name in axes:
        total *= lax.axis_size(name)
    copies = jnp.broadcast_to(own_source, (total,) + own_source.shape[1:])
    return lax.all_to_all(copies, axes, 0, 0, tiled=True)


def on_device(raw_traces):
    white = whiten(raw_traces)
    count = white.shape[0]
    sources = gather_sources(white[:1])
    recv = white.reshape(count, WINDOWS * 2 * NFREQ)
    src = sources.reshape(sources.shape[0], WINDOWS * 2 * NFREQ)
    lags_mid = correlate(recv, src, inverse_table(WLEN, NFREQ, MAXLAG), 2 * MAXLAG + 1)
    return jnp.transpose(lags_mid, (0, 2, 1))


def solution(mesh):
    return jax.shard_map(
        on_device,
        mesh=mesh,
        in_specs=(P(("grp", "mem"), None),),
        out_specs=P(("grp", "mem"), None, None),
        check_vma=False,
    )
```

```python
import functools
import math

import ml_dtypes
import numpy as np
import jax
import jax.numpy as jnp
from jax import lax
from jax.experimental import pallas as pl
from jax.sharding import PartitionSpec as P

CH_DEV = 8
WINDOWS = 2
WLEN = 1500
NFREQ = 384
TAPS = 32
MAXLAG = 200


def lowpass(taps):
    k = np.arange(taps, dtype=np.float64)
    centre = (taps - 1) / 2.0
    window = 0.5 - 0.5 * np.cos(2.0 * math.pi * (k + 0.5) / taps)
    return 0.5 * np.sinc((k - centre) * 0.5) * window


def forward_table(wlen, nfreq):
    times = np.arange(wlen, dtype=np.int64)
    bins = np.arange(1, nfreq + 1, dtype=np.int64)
    angle = 2.0 * math.pi * ((times[:, None] * bins[None, :]) % wlen) / wlen
    return np.concatenate([np.cos(angle), -np.sin(angle)], axis=1)


def filtered_table(wlen, nfreq, taps):
    filt = lowpass(taps)
    dft = forward_table(wlen, nfreq)
    table = np.zeros((2 * wlen + taps - 2, 2 * nfreq), np.float64)
    for k in range(taps):
        table[k : k + 2 * wlen : 2] += filt[k] * dft
    high = table.astype(np.float32).astype(ml_dtypes.bfloat16)
    low = (table - high.astype(np.float64)).astype(np.float32).astype(ml_dtypes.bfloat16)
    return jnp.asarray(high), jnp.asarray(low)


def split3(x):
    high = x.astype(jnp.bfloat16)
    rest = x - high.astype(jnp.float32)
    mid = rest.astype(jnp.bfloat16)
    low = (rest - mid.astype(jnp.float32)).astype(jnp.bfloat16)
    return high, mid, low


def inverse_table(wlen, nfreq, maxlag):
    bins = np.arange(1, nfreq + 1, dtype=np.int64)
    shifts = np.arange(2 * maxlag + 1, dtype=np.int64) - maxlag
    phase = np.mod(bins[:, None] * shifts[None, :], wlen).astype(np.float32)
    angle = np.float32(2.0 * math.pi) * phase / np.float32(wlen)
    table = np.concatenate([np.cos(angle), -np.sin(angle)], axis=0).astype(np.float32)
    padded = np.zeros((table.shape[0], -(-table.shape[1] // 128) * 128), np.float32)
    padded[:, : table.shape[1]] = table
    return jnp.asarray(padded).astype(jnp.bfloat16)


def whiten(raw_traces):
    count = raw_traces.shape[0]
    span = 2 * WLEN + TAPS - 2
    windows = jnp.stack(
        [raw_traces[:, w * 2 * WLEN : w * 2 * WLEN + span] for w in range(WINDOWS)], axis=1
    ).reshape(count * WINDOWS, span)
    rows = windows.shape[0]
    t_high, t_low = filtered_table(WLEN, NFREQ, TAPS)
    w_high, w_mid, w_low = split3(windows)
    by_high = jnp.dot(
        jnp.concatenate([w_high, w_mid, w_low], axis=0), t_high, preferred_element_type=jnp.float32
    )
    by_low = jnp.dot(jnp.concatenate([w_high, w_mid], axis=0), t_low, preferred_element_type=jnp.float32)
    spec = (by_high[:rows] + by_low[:rows]) + (
        (by_high[rows : 2 * rows] + by_low[rows:]) + by_high[2 * rows :]
    )
    spec_re = spec[:, :NFREQ]
    spec_im = spec[:, NFREQ:]
    power = spec_re * spec_re + spec_im * spec_im
    level = 0.01 * jnp.mean(power, axis=1, keepdims=True)
    factor = 1.0 / jnp.sqrt(power + level + 1e-06)
    white = jnp.concatenate([spec_re * factor, spec_im * factor], axis=1)
    return white.astype(jnp.bfloat16).reshape(count, WINDOWS, 2 * NFREQ)


SRC_BLOCK = 128


def correlate_kernel(scale, recv_ref, src_ref, table_ref, out_ref):
    nf = NFREQ
    src = src_ref[...].astype(jnp.float32)
    s_re0, s_im0 = src[:, 0:nf], src[:, nf : 2 * nf]
    s_re1, s_im1 = src[:, 2 * nf : 3 * nf], src[:, 3 * nf : 4 * nf]
    t_re = table_ref[0:nf, :]
    t_im = table_ref[nf : 2 * nf, :]
    lags = out_ref.shape[1]
    for c in range(out_ref.shape[0]):
        a = recv_ref[c : c + 1, :].astype(jnp.float32)
        a_re0, a_im0 = a[:, 0:nf], a[:, nf : 2 * nf]
        a_re1, a_im1 = a[:, 2 * nf : 3 * nf], a[:, 3 * nf : 4 * nf]
        c_re = (a_re0 * s_re0 + a_im0 * s_im0) + (a_re1 * s_re1 + a_im1 * s_im1)
        c_im = (a_im0 * s_re0 - a_re0 * s_im0) + (a_im1 * s_re1 - a_re1 * s_im1)
        acc = jnp.dot(c_re.astype(jnp.bfloat16), t_re, preferred_element_type=jnp.float32)
        acc = acc + jnp.dot(c_im.astype(jnp.bfloat16), t_im, preferred_element_type=jnp.float32)
        out_ref[c] = (acc.T[:lags] * scale).astype(out_ref.dtype)


def correlate(recv, src, table, lags):
    count, width = recv.shape[0], src.shape[0]
    block = min(SRC_BLOCK, width)
    scale = 1.0 / math.sqrt(WINDOWS * NFREQ)
    flops = 2 * count * width * table.shape[0] * table.shape[1] + 16 * count * width * NFREQ
    bytes_accessed = 2 * (recv.size + src.size + table.size + count * width * lags)
    return pl.pallas_call(
        functools.partial(correlate_kernel, scale),
        grid=(width // block,),
        in_specs=[
            pl.BlockSpec((count, recv.shape[1]), lambda j: (0, 0)),
            pl.BlockSpec((block, src.shape[1]), lambda j: (j, 0)),
            pl.BlockSpec(table.shape, lambda j: (0, 0)),
        ],
        out_specs=pl.BlockSpec((count, lags, block), lambda j: (0, 0, j)),
        out_shape=jax.ShapeDtypeStruct((count, lags, width), jnp.bfloat16),
        cost_estimate=pl.CostEstimate(flops=flops, transcendentals=0, bytes_accessed=bytes_accessed),
    )(recv, src, table)


def gather_sources(own_source):
    axes = ("grp", "mem")
    total = 1
    for name in axes:
        total *= lax.axis_size(name)
    copies = jnp.broadcast_to(own_source, (total,) + own_source.shape[1:])
    return lax.all_to_all(copies, axes, 0, 0, tiled=True)


def on_device(raw_traces):
    white = whiten(raw_traces)
    count = white.shape[0]
    sources = gather_sources(white[:1])
    recv = white.reshape(count, WINDOWS * 2 * NFREQ)
    src = sources.reshape(sources.shape[0], WINDOWS * 2 * NFREQ)
    lags_mid = correlate(recv, src, inverse_table(WLEN, NFREQ, MAXLAG), 2 * MAXLAG + 1)
    return jnp.transpose(lags_mid, (0, 2, 1))


def solution(mesh):
    return jax.shard_map(
        on_device,
        mesh=mesh,
        in_specs=(P(("grp", "mem"), None),),
        out_specs=P(("grp", "mem"), None, None),
        check_vma=False,
    )
```

```python
import functools
import math

import ml_dtypes
import numpy as np
import jax
import jax.numpy as jnp
from jax import lax
from jax.experimental import pallas as pl
from jax.sharding import PartitionSpec as P

CH_DEV = 8
WINDOWS = 2
WLEN = 1500
NFREQ = 384
TAPS = 32
MAXLAG = 200


def lowpass(taps):
    k = np.arange(taps, dtype=np.float64)
    centre = (taps - 1) / 2.0
    window = 0.5 - 0.5 * np.cos(2.0 * math.pi * (k + 0.5) / taps)
    return 0.5 * np.sinc((k - centre) * 0.5) * window


def forward_table(wlen, nfreq):
    times = np.arange(wlen, dtype=np.int64)
    bins = np.arange(1, nfreq + 1, dtype=np.int64)
    angle = 2.0 * math.pi * ((times[:, None] * bins[None, :]) % wlen) / wlen
    return np.concatenate([np.cos(angle), -np.sin(angle)], axis=1)


def filtered_table(wlen, nfreq, taps):
    filt = lowpass(taps)
    dft = forward_table(wlen, nfreq)
    table = np.zeros((2 * wlen + taps - 2, 2 * nfreq), np.float64)
    for k in range(taps):
        table[k : k + 2 * wlen : 2] += filt[k] * dft
    high = table.astype(np.float32).astype(ml_dtypes.bfloat16)
    low = (table - high.astype(np.float64)).astype(np.float32).astype(ml_dtypes.bfloat16)
    return jnp.asarray(high), jnp.asarray(low)


def to_bf16_grid(x):
    return lax.reduce_precision(x, exponent_bits=8, mantissa_bits=7)


def split3(x):
    high = to_bf16_grid(x)
    rest = x - high
    mid = to_bf16_grid(rest)
    low = rest - mid
    return high.astype(jnp.bfloat16), mid.astype(jnp.bfloat16), low.astype(jnp.bfloat16)


def inverse_table(wlen, nfreq, maxlag):
    bins = np.arange(1, nfreq + 1, dtype=np.int64)
    shifts = np.arange(2 * maxlag + 1, dtype=np.int64) - maxlag
    phase = np.mod(bins[:, None] * shifts[None, :], wlen).astype(np.float32)
    angle = np.float32(2.0 * math.pi) * phase / np.float32(wlen)
    table = np.concatenate([np.cos(angle), -np.sin(angle)], axis=0).astype(np.float32)
    padded = np.zeros((table.shape[0], -(-table.shape[1] // 128) * 128), np.float32)
    padded[:, : table.shape[1]] = table
    return jnp.asarray(padded).astype(jnp.bfloat16)


def whiten(raw_traces):
    count = raw_traces.shape[0]
    span = 2 * WLEN + TAPS - 2
    windows = jnp.stack(
        [raw_traces[:, w * 2 * WLEN : w * 2 * WLEN + span] for w in range(WINDOWS)], axis=1
    ).reshape(count * WINDOWS, span)
    rows = windows.shape[0]
    t_high, t_low = filtered_table(WLEN, NFREQ, TAPS)
    w_high, w_mid, w_low = split3(windows)
    by_high = jnp.dot(
        jnp.concatenate([w_high, w_mid, w_low], axis=0), t_high, preferred_element_type=jnp.float32
    )
    by_low = jnp.dot(jnp.concatenate([w_high, w_mid], axis=0), t_low, preferred_element_type=jnp.float32)
    spec = (by_high[:rows] + by_low[:rows]) + (
        (by_high[rows : 2 * rows] + by_low[rows:]) + by_high[2 * rows :]
    )
    spec_re = spec[:, :NFREQ]
    spec_im = spec[:, NFREQ:]
    power = spec_re * spec_re + spec_im * spec_im
    level = 0.01 * jnp.mean(power, axis=1, keepdims=True)
    factor = 1.0 / jnp.sqrt(power + level + 1e-06)
    white = jnp.concatenate([spec_re * factor, spec_im * factor], axis=1)
    return white.astype(jnp.bfloat16).reshape(count, WINDOWS, 2 * NFREQ)


SRC_BLOCK = 128


def correlate_kernel(scale, recv_ref, src_ref, table_ref, out_ref):
    nf = NFREQ
    src = src_ref[...].astype(jnp.float32)
    s_re0, s_im0 = src[:, 0:nf], src[:, nf : 2 * nf]
    s_re1, s_im1 = src[:, 2 * nf : 3 * nf], src[:, 3 * nf : 4 * nf]
    t_re = table_ref[0:nf, :]
    t_im = table_ref[nf : 2 * nf, :]
    lags = out_ref.shape[1]
    for c in range(out_ref.shape[0]):
        a = recv_ref[c : c + 1, :].astype(jnp.float32)
        a_re0, a_im0 = a[:, 0:nf], a[:, nf : 2 * nf]
        a_re1, a_im1 = a[:, 2 * nf : 3 * nf], a[:, 3 * nf : 4 * nf]
        c_re = (a_re0 * s_re0 + a_im0 * s_im0) + (a_re1 * s_re1 + a_im1 * s_im1)
        c_im = (a_im0 * s_re0 - a_re0 * s_im0) + (a_im1 * s_re1 - a_re1 * s_im1)
        acc = jnp.dot(c_re.astype(jnp.bfloat16), t_re, preferred_element_type=jnp.float32)
        acc = acc + jnp.dot(c_im.astype(jnp.bfloat16), t_im, preferred_element_type=jnp.float32)
        out_ref[c] = (acc.T[:lags] * scale).astype(out_ref.dtype)


def correlate(recv, src, table, lags):
    count, width = recv.shape[0], src.shape[0]
    block = min(SRC_BLOCK, width)
    scale = 1.0 / math.sqrt(WINDOWS * NFREQ)
    flops = 2 * count * width * table.shape[0] * table.shape[1] + 16 * count * width * NFREQ
    bytes_accessed = 2 * (recv.size + src.size + table.size + count * width * lags)
    return pl.pallas_call(
        functools.partial(correlate_kernel, scale),
        grid=(width // block,),
        in_specs=[
            pl.BlockSpec((count, recv.shape[1]), lambda j: (0, 0)),
            pl.BlockSpec((block, src.shape[1]), lambda j: (j, 0)),
            pl.BlockSpec(table.shape, lambda j: (0, 0)),
        ],
        out_specs=pl.BlockSpec((count, lags, block), lambda j: (0, 0, j)),
        out_shape=jax.ShapeDtypeStruct((count, lags, width), jnp.bfloat16),
        cost_estimate=pl.CostEstimate(flops=flops, transcendentals=0, bytes_accessed=bytes_accessed),
    )(recv, src, table)


def gather_sources(own_source):
    axes = ("grp", "mem")
    total = 1
    for name in axes:
        total *= lax.axis_size(name)
    copies = jnp.broadcast_to(own_source, (total,) + own_source.shape[1:])
    return lax.all_to_all(copies, axes, 0, 0, tiled=True)


def on_device(raw_traces):
    white = whiten(raw_traces)
    count = white.shape[0]
    sources = gather_sources(white[:1])
    recv = white.reshape(count, WINDOWS * 2 * NFREQ)
    src = sources.reshape(sources.shape[0], WINDOWS * 2 * NFREQ)
    lags_mid = correlate(recv, src, inverse_table(WLEN, NFREQ, MAXLAG), 2 * MAXLAG + 1)
    return jnp.transpose(lags_mid, (0, 2, 1))


def solution(mesh):
    return jax.shard_map(
        on_device,
        mesh=mesh,
        in_specs=(P(("grp", "mem"), None),),
        out_specs=P(("grp", "mem"), None, None),
        check_vma=False,
    )
```

```python
import functools
import math

import ml_dtypes
import numpy as np
import jax
import jax.numpy as jnp
from jax import lax
from jax.experimental import pallas as pl
from jax.sharding import PartitionSpec as P

CH_DEV = 8
WINDOWS = 2
WLEN = 1500
NFREQ = 384
TAPS = 32
MAXLAG = 200


def lowpass(taps):
    k = np.arange(taps, dtype=np.float64)
    centre = (taps - 1) / 2.0
    window = 0.5 - 0.5 * np.cos(2.0 * math.pi * (k + 0.5) / taps)
    return 0.5 * np.sinc((k - centre) * 0.5) * window


def forward_table(wlen, nfreq):
    times = np.arange(wlen, dtype=np.int64)
    bins = np.arange(1, nfreq + 1, dtype=np.int64)
    angle = 2.0 * math.pi * ((times[:, None] * bins[None, :]) % wlen) / wlen
    return np.concatenate([np.cos(angle), -np.sin(angle)], axis=1)


def filtered_table(wlen, nfreq, taps):
    filt = lowpass(taps)
    dft = forward_table(wlen, nfreq)
    table = np.zeros((2 * wlen + taps - 2, 2 * nfreq), np.float64)
    for k in range(taps):
        table[k : k + 2 * wlen : 2] += filt[k] * dft
    high = table.astype(np.float32).astype(ml_dtypes.bfloat16)
    low = (table - high.astype(np.float64)).astype(np.float32).astype(ml_dtypes.bfloat16)
    return jnp.asarray(high), jnp.asarray(low)


def to_bf16_grid(x):
    return lax.reduce_precision(x, exponent_bits=8, mantissa_bits=7)


def split3(x):
    high = to_bf16_grid(x)
    rest = x - high
    mid = to_bf16_grid(rest)
    low = rest - mid
    return high.astype(jnp.bfloat16), mid.astype(jnp.bfloat16), low.astype(jnp.bfloat16)


def inverse_table(wlen, nfreq, maxlag):
    bins = np.arange(1, nfreq + 1, dtype=np.int64)
    shifts = np.arange(2 * maxlag + 1, dtype=np.int64) - maxlag
    phase = np.mod(bins[:, None] * shifts[None, :], wlen).astype(np.float32)
    angle = np.float32(2.0 * math.pi) * phase / np.float32(wlen)
    table = np.concatenate([np.cos(angle), -np.sin(angle)], axis=0).astype(np.float32)
    padded = np.zeros((table.shape[0], -(-table.shape[1] // 128) * 128), np.float32)
    padded[:, : table.shape[1]] = table
    return jnp.asarray(padded).astype(jnp.bfloat16)


def whiten(raw_traces):
    count = raw_traces.shape[0]
    span = 2 * WLEN + TAPS - 2
    windows = jnp.stack(
        [raw_traces[:, w * 2 * WLEN : w * 2 * WLEN + span] for w in range(WINDOWS)], axis=1
    ).reshape(count * WINDOWS, span)
    rows = windows.shape[0]
    t_high, t_low = filtered_table(WLEN, NFREQ, TAPS)
    w_high, w_mid, w_low = split3(windows)
    by_high = jnp.dot(
        jnp.concatenate([w_high, w_mid, w_low], axis=0), t_high, preferred_element_type=jnp.float32
    )
    by_low = jnp.dot(jnp.concatenate([w_high, w_mid], axis=0), t_low, preferred_element_type=jnp.float32)
    spec = (by_high[:rows] + by_low[:rows]) + (
        (by_high[rows : 2 * rows] + by_low[rows:]) + by_high[2 * rows :]
    )
    spec_re = spec[:, :NFREQ]
    spec_im = spec[:, NFREQ:]
    power = spec_re * spec_re + spec_im * spec_im
    level = 0.01 * jnp.mean(power, axis=1, keepdims=True)
    factor = 1.0 / jnp.sqrt(power + level + 1e-06)
    white = jnp.concatenate([spec_re * factor, spec_im * factor], axis=1)
    return white.astype(jnp.bfloat16).reshape(count, WINDOWS, 2 * NFREQ)


SRC_BLOCK = 128


def correlate_kernel(scale, recv_ref, src_ref, table_ref, out_ref):
    nf = NFREQ
    src = src_ref[...].astype(jnp.float32)
    s_re0, s_im0 = src[:, 0:nf], src[:, nf : 2 * nf]
    s_re1, s_im1 = src[:, 2 * nf : 3 * nf], src[:, 3 * nf : 4 * nf]
    s_sum0, s_dif0 = s_re0 + s_im0, s_re0 - s_im0
    s_sum1, s_dif1 = s_re1 + s_im1, s_re1 - s_im1
    t_re = table_ref[0:nf, :]
    t_im = table_ref[nf : 2 * nf, :]
    lags = out_ref.shape[1]
    for c in range(out_ref.shape[0]):
        a = recv_ref[c : c + 1, :].astype(jnp.float32)
        a_re0, a_im0 = a[:, 0:nf], a[:, nf : 2 * nf]
        a_re1, a_im1 = a[:, 2 * nf : 3 * nf], a[:, 3 * nf : 4 * nf]
        k1_0 = s_re0 * (a_re0 + a_im0)
        k1_1 = s_re1 * (a_re1 + a_im1)
        c_re = (k1_0 - a_im0 * s_dif0) + (k1_1 - a_im1 * s_dif1)
        c_im = (k1_0 - a_re0 * s_sum0) + (k1_1 - a_re1 * s_sum1)
        acc = jnp.dot(c_re.astype(jnp.bfloat16), t_re, preferred_element_type=jnp.float32)
        acc = acc + jnp.dot(c_im.astype(jnp.bfloat16), t_im, preferred_element_type=jnp.float32)
        out_ref[c] = (acc.T[:lags] * scale).astype(out_ref.dtype)


def correlate(recv, src, table, lags):
    count, width = recv.shape[0], src.shape[0]
    block = min(SRC_BLOCK, width)
    scale = 1.0 / math.sqrt(WINDOWS * NFREQ)
    flops = 2 * count * width * table.shape[0] * table.shape[1] + 16 * count * width * NFREQ
    bytes_accessed = 2 * (recv.size + src.size + table.size + count * width * lags)
    return pl.pallas_call(
        functools.partial(correlate_kernel, scale),
        grid=(width // block,),
        in_specs=[
            pl.BlockSpec((count, recv.shape[1]), lambda j: (0, 0)),
            pl.BlockSpec((block, src.shape[1]), lambda j: (j, 0)),
            pl.BlockSpec(table.shape, lambda j: (0, 0)),
        ],
        out_specs=pl.BlockSpec((count, lags, block), lambda j: (0, 0, j)),
        out_shape=jax.ShapeDtypeStruct((count, lags, width), jnp.bfloat16),
        cost_estimate=pl.CostEstimate(flops=flops, transcendentals=0, bytes_accessed=bytes_accessed),
    )(recv, src, table)


def gather_sources(own_source):
    axes = ("grp", "mem")
    total = 1
    for name in axes:
        total *= lax.axis_size(name)
    copies = jnp.broadcast_to(own_source, (total,) + own_source.shape[1:])
    return lax.all_to_all(copies, axes, 0, 0, tiled=True)


def on_device(raw_traces):
    white = whiten(raw_traces)
    count = white.shape[0]
    sources = gather_sources(white[:1])
    recv = white.reshape(count, WINDOWS * 2 * NFREQ)
    src = sources.reshape(sources.shape[0], WINDOWS * 2 * NFREQ)
    lags_mid = correlate(recv, src, inverse_table(WLEN, NFREQ, MAXLAG), 2 * MAXLAG + 1)
    return jnp.transpose(lags_mid, (0, 2, 1))


def solution(mesh):
    return jax.shard_map(
        on_device,
        mesh=mesh,
        in_specs=(P(("grp", "mem"), None),),
        out_specs=P(("grp", "mem"), None, None),
        check_vma=False,
    )
```

```python
import functools
import math

import ml_dtypes
import numpy as np
import jax
import jax.numpy as jnp
from jax import lax
from jax.experimental import pallas as pl
from jax.sharding import PartitionSpec as P

CH_DEV = 8
WINDOWS = 2
WLEN = 1500
NFREQ = 384
TAPS = 32
MAXLAG = 200


def lowpass(taps):
    k = np.arange(taps, dtype=np.float64)
    centre = (taps - 1) / 2.0
    window = 0.5 - 0.5 * np.cos(2.0 * math.pi * (k + 0.5) / taps)
    return 0.5 * np.sinc((k - centre) * 0.5) * window


def forward_table(wlen, nfreq):
    times = np.arange(wlen, dtype=np.int64)
    bins = np.arange(1, nfreq + 1, dtype=np.int64)
    angle = 2.0 * math.pi * ((times[:, None] * bins[None, :]) % wlen) / wlen
    return np.concatenate([np.cos(angle), -np.sin(angle)], axis=1)


def filtered_table(wlen, nfreq, taps):
    filt = lowpass(taps)
    dft = forward_table(wlen, nfreq)
    table = np.zeros((2 * wlen + taps - 2, 2 * nfreq), np.float64)
    for k in range(taps):
        table[k : k + 2 * wlen : 2] += filt[k] * dft
    high = table.astype(np.float32).astype(ml_dtypes.bfloat16)
    low = (table - high.astype(np.float64)).astype(np.float32).astype(ml_dtypes.bfloat16)
    return jnp.asarray(high), jnp.asarray(low)


def to_bf16_grid(x):
    return lax.reduce_precision(x, exponent_bits=8, mantissa_bits=7)


def split3(x):
    high = to_bf16_grid(x)
    rest = x - high
    mid = to_bf16_grid(rest)
    low = rest - mid
    return high.astype(jnp.bfloat16), mid.astype(jnp.bfloat16), low.astype(jnp.bfloat16)


def inverse_table(wlen, nfreq, maxlag):
    bins = np.arange(1, nfreq + 1, dtype=np.int64)
    shifts = np.arange(2 * maxlag + 1, dtype=np.int64) - maxlag
    phase = np.mod(bins[:, None] * shifts[None, :], wlen).astype(np.float32)
    angle = np.float32(2.0 * math.pi) * phase / np.float32(wlen)
    table = np.concatenate([np.cos(angle), -np.sin(angle)], axis=0).astype(np.float32)
    padded = np.zeros((table.shape[0], -(-table.shape[1] // 128) * 128), np.float32)
    padded[:, : table.shape[1]] = table
    return jnp.asarray(padded).astype(jnp.bfloat16)


def whiten(raw_traces):
    count = raw_traces.shape[0]
    span = 2 * WLEN + TAPS - 2
    windows = jnp.stack(
        [raw_traces[:, w * 2 * WLEN : w * 2 * WLEN + span] for w in range(WINDOWS)], axis=1
    ).reshape(count * WINDOWS, span)
    rows = windows.shape[0]
    t_high, t_low = filtered_table(WLEN, NFREQ, TAPS)
    w_high, w_mid, w_low = split3(windows)
    by_high = jnp.dot(
        jnp.concatenate([w_high, w_mid, w_low], axis=0), t_high, preferred_element_type=jnp.float32
    )
    by_low = jnp.dot(jnp.concatenate([w_high, w_mid], axis=0), t_low, preferred_element_type=jnp.float32)
    spec = (by_high[:rows] + by_low[:rows]) + (
        (by_high[rows : 2 * rows] + by_low[rows:]) + by_high[2 * rows :]
    )
    spec_re = spec[:, :NFREQ]
    spec_im = spec[:, NFREQ:]
    power = spec_re * spec_re + spec_im * spec_im
    level = 0.01 * jnp.mean(power, axis=1, keepdims=True)
    factor = 1.0 / jnp.sqrt(power + level + 1e-06)
    white = jnp.concatenate([spec_re * factor, spec_im * factor], axis=1)
    return white.astype(jnp.bfloat16).reshape(count, WINDOWS, 2 * NFREQ)


SRC_BLOCK = 128


def correlate_kernel(scale, recv_ref, src_ref, table_ref, out_ref):
    nf = NFREQ
    s0 = src_ref[:, 0, :].astype(jnp.float32)
    s1 = src_ref[:, 1, :].astype(jnp.float32)
    s_re0, s_im0 = s0[:, 0:nf], s0[:, nf : 2 * nf]
    s_re1, s_im1 = s1[:, 0:nf], s1[:, nf : 2 * nf]
    t_re = table_ref[0:nf, :]
    t_im = table_ref[nf : 2 * nf, :]
    lags = out_ref.shape[1]
    for c in range(out_ref.shape[0]):
        a = recv_ref[c : c + 1, :].astype(jnp.float32)
        a_re0, a_im0 = a[:, 0:nf], a[:, nf : 2 * nf]
        a_re1, a_im1 = a[:, 2 * nf : 3 * nf], a[:, 3 * nf : 4 * nf]
        c_re = (a_re0 * s_re0 + a_im0 * s_im0) + (a_re1 * s_re1 + a_im1 * s_im1)
        c_im = (a_im0 * s_re0 - a_re0 * s_im0) + (a_im1 * s_re1 - a_re1 * s_im1)
        acc = jnp.dot(c_re.astype(jnp.bfloat16), t_re, preferred_element_type=jnp.float32)
        acc = acc + jnp.dot(c_im.astype(jnp.bfloat16), t_im, preferred_element_type=jnp.float32)
        out_ref[c] = (acc.T[:lags] * scale).astype(out_ref.dtype)


def correlate(recv, src, table, lags):
    count, width = recv.shape[0], src.shape[0]
    block = min(SRC_BLOCK, width)
    scale = 1.0 / math.sqrt(WINDOWS * NFREQ)
    flops = 2 * count * width * table.shape[0] * table.shape[1] + 16 * count * width * NFREQ
    bytes_accessed = 2 * (recv.size + src.size + table.size + count * width * lags)
    return pl.pallas_call(
        functools.partial(correlate_kernel, scale),
        grid=(width // block,),
        in_specs=[
            pl.BlockSpec((count, recv.shape[1]), lambda j: (0, 0)),
            pl.BlockSpec((block,) + src.shape[1:], lambda j: (j, 0, 0)),
            pl.BlockSpec(table.shape, lambda j: (0, 0)),
        ],
        out_specs=pl.BlockSpec((count, lags, block), lambda j: (0, 0, j)),
        out_shape=jax.ShapeDtypeStruct((count, lags, width), jnp.bfloat16),
        cost_estimate=pl.CostEstimate(flops=flops, transcendentals=0, bytes_accessed=bytes_accessed),
    )(recv, src, table)


def gather_sources(own_source):
    axes = ("grp", "mem")
    total = 1
    for name in axes:
        total *= lax.axis_size(name)
    copies = jnp.broadcast_to(own_source, (total,) + own_source.shape[1:])
    return lax.all_to_all(copies, axes, 0, 0, tiled=True)


def on_device(raw_traces):
    white = whiten(raw_traces)
    count = white.shape[0]
    sources = gather_sources(white[:1])
    recv = white.reshape(count, WINDOWS * 2 * NFREQ)
    src = sources
    lags_mid = correlate(recv, src, inverse_table(WLEN, NFREQ, MAXLAG), 2 * MAXLAG + 1)
    return jnp.transpose(lags_mid, (0, 2, 1))


def solution(mesh):
    return jax.shard_map(
        on_device,
        mesh=mesh,
        in_specs=(P(("grp", "mem"), None),),
        out_specs=P(("grp", "mem"), None, None),
        check_vma=False,
    )
```

```python
import functools
import math

import ml_dtypes
import numpy as np
import jax
import jax.numpy as jnp
from jax import lax
from jax.experimental import pallas as pl
from jax.sharding import PartitionSpec as P

CH_DEV = 8
WINDOWS = 2
WLEN = 1500
NFREQ = 384
TAPS = 32
MAXLAG = 200


def lowpass(taps):
    k = np.arange(taps, dtype=np.float64)
    centre = (taps - 1) / 2.0
    window = 0.5 - 0.5 * np.cos(2.0 * math.pi * (k + 0.5) / taps)
    return 0.5 * np.sinc((k - centre) * 0.5) * window


def forward_table(wlen, nfreq):
    times = np.arange(wlen, dtype=np.int64)
    bins = np.arange(1, nfreq + 1, dtype=np.int64)
    angle = 2.0 * math.pi * ((times[:, None] * bins[None, :]) % wlen) / wlen
    return np.concatenate([np.cos(angle), -np.sin(angle)], axis=1)


def filtered_table(wlen, nfreq, taps):
    filt = lowpass(taps)
    dft = forward_table(wlen, nfreq)
    table = np.zeros((2 * wlen + taps - 2, 2 * nfreq), np.float64)
    for k in range(taps):
        table[k : k + 2 * wlen : 2] += filt[k] * dft
    high = table.astype(np.float32).astype(ml_dtypes.bfloat16)
    low = (table - high.astype(np.float64)).astype(np.float32).astype(ml_dtypes.bfloat16)
    return jnp.asarray(high), jnp.asarray(low)


def to_bf16_grid(x):
    return lax.reduce_precision(x, exponent_bits=8, mantissa_bits=7)


def split3(x):
    high = to_bf16_grid(x)
    rest = x - high
    mid = to_bf16_grid(rest)
    low = rest - mid
    return high.astype(jnp.bfloat16), mid.astype(jnp.bfloat16), low.astype(jnp.bfloat16)


def inverse_table(wlen, nfreq, maxlag):
    bins = np.arange(1, nfreq + 1, dtype=np.int64)
    shifts = np.arange(2 * maxlag + 1, dtype=np.int64) - maxlag
    phase = np.mod(bins[:, None] * shifts[None, :], wlen).astype(np.float32)
    angle = np.float32(2.0 * math.pi) * phase / np.float32(wlen)
    table = np.concatenate([np.cos(angle), -np.sin(angle)], axis=0).astype(np.float32)
    padded = np.zeros((table.shape[0], -(-table.shape[1] // 128) * 128), np.float32)
    padded[:, : table.shape[1]] = table
    return jnp.asarray(padded).astype(jnp.bfloat16)


def whiten(raw_traces):
    count = raw_traces.shape[0]
    span = 2 * WLEN + TAPS - 2
    windows = jnp.stack(
        [raw_traces[:, w * 2 * WLEN : w * 2 * WLEN + span] for w in range(WINDOWS)], axis=1
    ).reshape(count * WINDOWS, span)
    rows = windows.shape[0]
    t_high, t_low = filtered_table(WLEN, NFREQ, TAPS)
    w_high, w_mid, w_low = split3(windows)
    by_high = jnp.dot(
        jnp.concatenate([w_high, w_mid, w_low], axis=0), t_high, preferred_element_type=jnp.float32
    )
    by_low = jnp.dot(jnp.concatenate([w_high, w_mid], axis=0), t_low, preferred_element_type=jnp.float32)
    spec = (by_high[:rows] + by_low[:rows]) + (
        (by_high[rows : 2 * rows] + by_low[rows:]) + by_high[2 * rows :]
    )
    spec_re = spec[:, :NFREQ]
    spec_im = spec[:, NFREQ:]
    power = spec_re * spec_re + spec_im * spec_im
    level = 0.01 * jnp.mean(power, axis=1, keepdims=True)
    factor = 1.0 / jnp.sqrt(power + level + 1e-06)
    white = jnp.concatenate([spec_re * factor, spec_im * factor], axis=1)
    return white.astype(jnp.bfloat16).reshape(count, WINDOWS, 2 * NFREQ)


SRC_BLOCK = 256


def correlate_kernel(scale, recv_ref, src_ref, table_ref, out_ref):
    nf = NFREQ
    src = src_ref[...].astype(jnp.float32)
    s_re0, s_im0 = src[:, 0:nf], src[:, nf : 2 * nf]
    s_re1, s_im1 = src[:, 2 * nf : 3 * nf], src[:, 3 * nf : 4 * nf]
    t_re = table_ref[0:nf, :]
    t_im = table_ref[nf : 2 * nf, :]
    lags = out_ref.shape[1]
    for c in range(out_ref.shape[0]):
        a = recv_ref[c : c + 1, :].astype(jnp.float32)
        a_re0, a_im0 = a[:, 0:nf], a[:, nf : 2 * nf]
        a_re1, a_im1 = a[:, 2 * nf : 3 * nf], a[:, 3 * nf : 4 * nf]
        c_re = (a_re0 * s_re0 + a_im0 * s_im0) + (a_re1 * s_re1 + a_im1 * s_im1)
        c_im = (a_im0 * s_re0 - a_re0 * s_im0) + (a_im1 * s_re1 - a_re1 * s_im1)
        acc = jnp.dot(c_re.astype(jnp.bfloat16), t_re, preferred_element_type=jnp.float32)
        acc = acc + jnp.dot(c_im.astype(jnp.bfloat16), t_im, preferred_element_type=jnp.float32)
        out_ref[c] = (acc.T[:lags] * scale).astype(out_ref.dtype)


def correlate(recv, src, table, lags):
    count, width = recv.shape[0], src.shape[0]
    block = min(SRC_BLOCK, width)
    scale = 1.0 / math.sqrt(WINDOWS * NFREQ)
    flops = 2 * count * width * table.shape[0] * table.shape[1] + 16 * count * width * NFREQ
    bytes_accessed = 2 * (recv.size + src.size + table.size + count * width * lags)
    return pl.pallas_call(
        functools.partial(correlate_kernel, scale),
        grid=(width // block,),
        in_specs=[
            pl.BlockSpec((count, recv.shape[1]), lambda j: (0, 0)),
            pl.BlockSpec((block, src.shape[1]), lambda j: (j, 0)),
            pl.BlockSpec(table.shape, lambda j: (0, 0)),
        ],
        out_specs=pl.BlockSpec((count, lags, block), lambda j: (0, 0, j)),
        out_shape=jax.ShapeDtypeStruct((count, lags, width), jnp.bfloat16),
        cost_estimate=pl.CostEstimate(flops=flops, transcendentals=0, bytes_accessed=bytes_accessed),
    )(recv, src, table)


def gather_sources(own_source):
    axes = ("grp", "mem")
    total = 1
    for name in axes:
        total *= lax.axis_size(name)
    copies = jnp.broadcast_to(own_source, (total,) + own_source.shape[1:])
    return lax.all_to_all(copies, axes, 0, 0, tiled=True)


def on_device(raw_traces):
    white = whiten(raw_traces)
    count = white.shape[0]
    sources = gather_sources(white[:1])
    recv = white.reshape(count, WINDOWS * 2 * NFREQ)
    src = sources.reshape(sources.shape[0], WINDOWS * 2 * NFREQ)
    lags_mid = correlate(recv, src, inverse_table(WLEN, NFREQ, MAXLAG), 2 * MAXLAG + 1)
    return jnp.transpose(lags_mid, (0, 2, 1))


def solution(mesh):
    return jax.shard_map(
        on_device,
        mesh=mesh,
        in_specs=(P(("grp", "mem"), None),),
        out_specs=P(("grp", "mem"), None, None),
        check_vma=False,
    )
```

```python
import functools
import math

import ml_dtypes
import numpy as np
import jax
import jax.numpy as jnp
from jax import lax
from jax.experimental import pallas as pl
from jax.sharding import PartitionSpec as P

CH_DEV = 8
WINDOWS = 2
WLEN = 1500
NFREQ = 384
TAPS = 32
MAXLAG = 200


def lowpass(taps):
    k = np.arange(taps, dtype=np.float64)
    centre = (taps - 1) / 2.0
    window = 0.5 - 0.5 * np.cos(2.0 * math.pi * (k + 0.5) / taps)
    return 0.5 * np.sinc((k - centre) * 0.5) * window


def forward_table(wlen, nfreq):
    times = np.arange(wlen, dtype=np.int64)
    bins = np.arange(1, nfreq + 1, dtype=np.int64)
    angle = 2.0 * math.pi * ((times[:, None] * bins[None, :]) % wlen) / wlen
    return np.concatenate([np.cos(angle), -np.sin(angle)], axis=1)


def filtered_table(wlen, nfreq, taps):
    filt = lowpass(taps)
    dft = forward_table(wlen, nfreq)
    table = np.zeros((2 * wlen + taps - 2, 2 * nfreq), np.float64)
    for k in range(taps):
        table[k : k + 2 * wlen : 2] += filt[k] * dft
    high = table.astype(np.float32).astype(ml_dtypes.bfloat16)
    low = (table - high.astype(np.float64)).astype(np.float32).astype(ml_dtypes.bfloat16)
    return jnp.asarray(high), jnp.asarray(low)


def to_bf16_grid(x):
    return lax.reduce_precision(x, exponent_bits=8, mantissa_bits=7)


def split3(x):
    high = to_bf16_grid(x)
    rest = x - high
    mid = to_bf16_grid(rest)
    low = rest - mid
    return high.astype(jnp.bfloat16), mid.astype(jnp.bfloat16), low.astype(jnp.bfloat16)


def inverse_table(wlen, nfreq, maxlag):
    bins = np.arange(1, nfreq + 1, dtype=np.int64)
    shifts = np.arange(2 * maxlag + 1, dtype=np.int64) - maxlag
    phase = np.mod(bins[:, None] * shifts[None, :], wlen).astype(np.float32)
    angle = np.float32(2.0 * math.pi) * phase / np.float32(wlen)
    table = np.concatenate([np.cos(angle), -np.sin(angle)], axis=0).astype(np.float32)
    padded = np.zeros((table.shape[0], -(-table.shape[1] // 128) * 128), np.float32)
    padded[:, : table.shape[1]] = table
    return jnp.asarray(padded).astype(jnp.bfloat16)


def whiten(raw_traces):
    count = raw_traces.shape[0]
    span = 2 * WLEN + TAPS - 2
    windows = jnp.stack(
        [raw_traces[:, w * 2 * WLEN : w * 2 * WLEN + span] for w in range(WINDOWS)], axis=1
    ).reshape(count * WINDOWS, span)
    rows = windows.shape[0]
    t_high, t_low = filtered_table(WLEN, NFREQ, TAPS)
    w_high, w_mid, w_low = split3(windows)
    by_high = jnp.dot(
        jnp.concatenate([w_high, w_mid, w_low], axis=0), t_high, preferred_element_type=jnp.float32
    )
    by_low = jnp.dot(jnp.concatenate([w_high, w_mid], axis=0), t_low, preferred_element_type=jnp.float32)
    spec = (by_high[:rows] + by_low[:rows]) + (
        (by_high[rows : 2 * rows] + by_low[rows:]) + by_high[2 * rows :]
    )
    spec_re = spec[:, :NFREQ]
    spec_im = spec[:, NFREQ:]
    power = spec_re * spec_re + spec_im * spec_im
    level = 0.01 * jnp.mean(power, axis=1, keepdims=True)
    factor = 1.0 / jnp.sqrt(power + level + 1e-06)
    white = jnp.concatenate([spec_re * factor, spec_im * factor], axis=1)
    return white.astype(jnp.bfloat16).reshape(count, WINDOWS, 2 * NFREQ)


SRC_BLOCK = 256


def correlate_kernel(scale, recv_ref, src_ref, table_ref, out_ref):
    nf = NFREQ
    src = src_ref[...].astype(jnp.float32)
    s_re0, s_im0 = src[:, 0:nf], src[:, nf : 2 * nf]
    s_re1, s_im1 = src[:, 2 * nf : 3 * nf], src[:, 3 * nf : 4 * nf]
    t_re = table_ref[0:nf, :]
    t_im = table_ref[nf : 2 * nf, :]
    lags = out_ref.shape[0]
    results = []
    for c in range(out_ref.shape[1]):
        a = recv_ref[c : c + 1, :].astype(jnp.float32)
        a_re0, a_im0 = a[:, 0:nf], a[:, nf : 2 * nf]
        a_re1, a_im1 = a[:, 2 * nf : 3 * nf], a[:, 3 * nf : 4 * nf]
        c_re = (a_re0 * s_re0 + a_im0 * s_im0) + (a_re1 * s_re1 + a_im1 * s_im1)
        c_im = (a_im0 * s_re0 - a_re0 * s_im0) + (a_im1 * s_re1 - a_re1 * s_im1)
        acc = jnp.dot(c_re.astype(jnp.bfloat16), t_re, preferred_element_type=jnp.float32)
        acc = acc + jnp.dot(c_im.astype(jnp.bfloat16), t_im, preferred_element_type=jnp.float32)
        results.append(acc.T[:lags] * scale)
    out_ref[...] = jnp.stack(results, axis=1).astype(out_ref.dtype)


def correlate(recv, src, table, lags):
    count, width = recv.shape[0], src.shape[0]
    block = min(SRC_BLOCK, width)
    scale = 1.0 / math.sqrt(WINDOWS * NFREQ)
    flops = 2 * count * width * table.shape[0] * table.shape[1] + 16 * count * width * NFREQ
    bytes_accessed = 2 * (recv.size + src.size + table.size + count * width * lags)
    return pl.pallas_call(
        functools.partial(correlate_kernel, scale),
        grid=(width // block,),
        in_specs=[
            pl.BlockSpec((count, recv.shape[1]), lambda j: (0, 0)),
            pl.BlockSpec((block, src.shape[1]), lambda j: (j, 0)),
            pl.BlockSpec(table.shape, lambda j: (0, 0)),
        ],
        out_specs=pl.BlockSpec((lags, count, block), lambda j: (0, 0, j)),
        out_shape=jax.ShapeDtypeStruct((lags, count, width), jnp.bfloat16),
        cost_estimate=pl.CostEstimate(flops=flops, transcendentals=0, bytes_accessed=bytes_accessed),
    )(recv, src, table)


def gather_sources(own_source):
    axes = ("grp", "mem")
    total = 1
    for name in axes:
        total *= lax.axis_size(name)
    copies = jnp.broadcast_to(own_source, (total,) + own_source.shape[1:])
    return lax.all_to_all(copies, axes, 0, 0, tiled=True)


def on_device(raw_traces):
    white = whiten(raw_traces)
    count = white.shape[0]
    sources = gather_sources(white[:1])
    recv = white.reshape(count, WINDOWS * 2 * NFREQ)
    src = sources.reshape(sources.shape[0], WINDOWS * 2 * NFREQ)
    lags_mid = correlate(recv, src, inverse_table(WLEN, NFREQ, MAXLAG), 2 * MAXLAG + 1)
    return jnp.transpose(lags_mid, (1, 2, 0))


def solution(mesh):
    return jax.shard_map(
        on_device,
        mesh=mesh,
        in_specs=(P(("grp", "mem"), None),),
        out_specs=P(("grp", "mem"), None, None),
        check_vma=False,
    )
```

```python
import functools
import math

import ml_dtypes
import numpy as np
import jax
import jax.numpy as jnp
from jax import lax
from jax.experimental import pallas as pl
from jax.sharding import PartitionSpec as P

CH_DEV = 8
WINDOWS = 2
WLEN = 1500
NFREQ = 384
TAPS = 32
MAXLAG = 200


def lowpass(taps):
    k = np.arange(taps, dtype=np.float64)
    centre = (taps - 1) / 2.0
    window = 0.5 - 0.5 * np.cos(2.0 * math.pi * (k + 0.5) / taps)
    return 0.5 * np.sinc((k - centre) * 0.5) * window


def forward_table(wlen, nfreq):
    times = np.arange(wlen, dtype=np.int64)
    bins = np.arange(1, nfreq + 1, dtype=np.int64)
    angle = 2.0 * math.pi * ((times[:, None] * bins[None, :]) % wlen) / wlen
    return np.concatenate([np.cos(angle), -np.sin(angle)], axis=1)


def filtered_table(wlen, nfreq, taps):
    filt = lowpass(taps)
    dft = forward_table(wlen, nfreq)
    table = np.zeros((2 * wlen + taps - 2, 2 * nfreq), np.float64)
    for k in range(taps):
        table[k : k + 2 * wlen : 2] += filt[k] * dft
    high = table.astype(np.float32).astype(ml_dtypes.bfloat16)
    low = (table - high.astype(np.float64)).astype(np.float32).astype(ml_dtypes.bfloat16)
    return jnp.asarray(high), jnp.asarray(low)


def to_bf16_grid(x):
    return lax.reduce_precision(x, exponent_bits=8, mantissa_bits=7)


def split3(x):
    high = to_bf16_grid(x)
    rest = x - high
    mid = to_bf16_grid(rest)
    low = rest - mid
    return high.astype(jnp.bfloat16), mid.astype(jnp.bfloat16), low.astype(jnp.bfloat16)


def inverse_table(wlen, nfreq, maxlag):
    bins = np.arange(1, nfreq + 1, dtype=np.int64)
    shifts = np.arange(2 * maxlag + 1, dtype=np.int64) - maxlag
    phase = np.mod(bins[:, None] * shifts[None, :], wlen).astype(np.float32)
    angle = np.float32(2.0 * math.pi) * phase / np.float32(wlen)
    table = np.concatenate([np.cos(angle), -np.sin(angle)], axis=0).astype(np.float32)
    padded = np.zeros((table.shape[0], -(-table.shape[1] // 128) * 128), np.float32)
    padded[:, : table.shape[1]] = table
    return jnp.asarray(padded).astype(jnp.bfloat16)


def whiten(raw_traces):
    count = raw_traces.shape[0]
    span = 2 * WLEN + TAPS - 2
    windows = jnp.stack(
        [raw_traces[:, w * 2 * WLEN : w * 2 * WLEN + span] for w in range(WINDOWS)], axis=1
    ).reshape(count * WINDOWS, span)
    rows = windows.shape[0]
    t_high, t_low = filtered_table(WLEN, NFREQ, TAPS)
    w_high, w_mid, w_low = split3(windows)
    by_high = jnp.dot(
        jnp.concatenate([w_high, w_mid, w_low], axis=0), t_high, preferred_element_type=jnp.float32
    )
    by_low = jnp.dot(jnp.concatenate([w_high, w_mid], axis=0), t_low, preferred_element_type=jnp.float32)
    spec = (by_high[:rows] + by_low[:rows]) + (
        (by_high[rows : 2 * rows] + by_low[rows:]) + by_high[2 * rows :]
    )
    spec_re = spec[:, :NFREQ]
    spec_im = spec[:, NFREQ:]
    power = spec_re * spec_re + spec_im * spec_im
    level = 0.01 * jnp.mean(power, axis=1, keepdims=True)
    factor = 1.0 / jnp.sqrt(power + level + 1e-06)
    white = jnp.concatenate([spec_re * factor, spec_im * factor], axis=1)
    return white.astype(jnp.bfloat16).reshape(count, WINDOWS, 2 * NFREQ)


SRC_BLOCK = 512


def correlate_kernel(scale, recv_ref, src_ref, table_ref, out_ref):
    nf = NFREQ
    src = src_ref[...].astype(jnp.float32)
    s_re0, s_im0 = src[:, 0:nf], src[:, nf : 2 * nf]
    s_re1, s_im1 = src[:, 2 * nf : 3 * nf], src[:, 3 * nf : 4 * nf]
    t_re = table_ref[0:nf, :]
    t_im = table_ref[nf : 2 * nf, :]
    lags = out_ref.shape[1]
    for c in range(out_ref.shape[0]):
        a = recv_ref[c : c + 1, :].astype(jnp.float32)
        a_re0, a_im0 = a[:, 0:nf], a[:, nf : 2 * nf]
        a_re1, a_im1 = a[:, 2 * nf : 3 * nf], a[:, 3 * nf : 4 * nf]
        c_re = (a_re0 * s_re0 + a_im0 * s_im0) + (a_re1 * s_re1 + a_im1 * s_im1)
        c_im = (a_im0 * s_re0 - a_re0 * s_im0) + (a_im1 * s_re1 - a_re1 * s_im1)
        acc = jnp.dot(c_re.astype(jnp.bfloat16), t_re, preferred_element_type=jnp.float32)
        acc = acc + jnp.dot(c_im.astype(jnp.bfloat16), t_im, preferred_element_type=jnp.float32)
        out_ref[c] = (acc.T[:lags] * scale).astype(out_ref.dtype)


def correlate(recv, src, table, lags):
    count, width = recv.shape[0], src.shape[0]
    block = min(SRC_BLOCK, width)
    scale = 1.0 / math.sqrt(WINDOWS * NFREQ)
    flops = 2 * count * width * table.shape[0] * table.shape[1] + 16 * count * width * NFREQ
    bytes_accessed = 2 * (recv.size + src.size + table.size + count * width * lags)
    return pl.pallas_call(
        functools.partial(correlate_kernel, scale),
        grid=(width // block,),
        in_specs=[
            pl.BlockSpec((count, recv.shape[1]), lambda j: (0, 0)),
            pl.BlockSpec((block, src.shape[1]), lambda j: (j, 0)),
            pl.BlockSpec(table.shape, lambda j: (0, 0)),
        ],
        out_specs=pl.BlockSpec((count, lags, block), lambda j: (0, 0, j)),
        out_shape=jax.ShapeDtypeStruct((count, lags, width), jnp.bfloat16),
        cost_estimate=pl.CostEstimate(flops=flops, transcendentals=0, bytes_accessed=bytes_accessed),
    )(recv, src, table)


def gather_sources(own_source):
    axes = ("grp", "mem")
    total = 1
    for name in axes:
        total *= lax.axis_size(name)
    copies = jnp.broadcast_to(own_source, (total,) + own_source.shape[1:])
    return lax.all_to_all(copies, axes, 0, 0, tiled=True)


def on_device(raw_traces):
    white = whiten(raw_traces)
    count = white.shape[0]
    sources = gather_sources(white[:1])
    recv = white.reshape(count, WINDOWS * 2 * NFREQ)
    src = sources.reshape(sources.shape[0], WINDOWS * 2 * NFREQ)
    lags_mid = correlate(recv, src, inverse_table(WLEN, NFREQ, MAXLAG), 2 * MAXLAG + 1)
    return jnp.transpose(lags_mid, (0, 2, 1))


def solution(mesh):
    return jax.shard_map(
        on_device,
        mesh=mesh,
        in_specs=(P(("grp", "mem"), None),),
        out_specs=P(("grp", "mem"), None, None),
        check_vma=False,
    )
```
